512 devices in a mesh: pipe: 16 (over z_hi, y), zero: 32 (over z_lo, x, core).
Axes of the slice: x: 4, y: 4, z: 16 (z_hi: 4, z_lo: 4; z = z_hi * 4 + z_lo), core: 2. Of those that a mesh axis runs over, the one named last changes fastest.
Arguments:
- residual: bfloat16 [16, 2048, 4096], P('pipe', 'zero'), may hold values from -6 to 6
- norm_gain: bfloat16 [16, 4096], P('pipe'), may hold values from 0.099609375 to 1.8984375
- queries: bfloat16 [16, 2048, 4096], P('pipe', 'zero'), may hold values from -74 to 74
- cached_kv: bfloat16 [16, 512, 1024], P('pipe', 'zero'), may hold values from -6 to 6
- panel_blocks: bfloat16 [16, 160, 128, 128], P('pipe', 'zero'), may hold values from -0.125 to 0.125
- block_rows: int32 [16, 8, 20], P('pipe'), may hold values from 0 to 31, as said below
- counts: int32 [16, 8], P('pipe'), may hold values from 12 to 20, as said below
Outputs:
- passed: bfloat16 [16, 2048, 4096], P('pipe', 'zero')
- new_kv: bfloat16 [16, 2048, 1024], P('pipe', 'zero')
The draws below stay inside these ranges and needn't reach their ends.
Inputs may be any that keep to these rules, and one draw needn't show every extreme that they name: `block_rows`: row blocks named by the slots of one panel are all different. `counts`: slots at or beyond a panel's count are padding.
All inputs are finite; a program needn't handle non-finite values.
Results may differ from the reference program's by a relative error of at most 0.0047.
The reference program's roundings to bfloat16 on the way count: a program that leaves them out, or rounds other values in their place, can miss the bound.
Values may be sent and summed in bfloat16 or wider, within the bound.
No kernel may reach another device: no remote copies, remote signals or barrier semaphores. Data moves between devices by JAX's collectives and lax.ppermute only.
A program may use at most 64 MiB of HBM per device.

```python
import math
import jax
import jax.numpy as jnp
from jax import lax

D = 4096
QH = 32
KVH = 4
HD = 128
BLOCK = 128
CAP = 20
SECTIONS = 16
STRETCH = 2048
CACHE = 512
GROUP = 8
NB = 32
PANELS = 8


def cache_values(key):
    raw_key = jax.random.fold_in(key, 11)
    shape = (SECTIONS, CACHE, 2 * KVH * HD)
    cache_vals = jnp.clip(jax.random.normal(raw_key, shape, jnp.float32), -6.0, 6.0)
    return cache_vals


def draw_cached_kv(key, part):
    return cache_values(key).astype(jnp.bfloat16)


def draw_queries(key, part):
    raw_key = jax.random.fold_in(key, 13)
    shape = (SECTIONS, STRETCH, QH * HD)
    edge_value = 64.0 + float(1300 // HD)
    query_vals = jnp.clip(jax.random.normal(raw_key, shape, jnp.float32), -6.0, 6.0)
    query_vals = query_vals.at[:, STRETCH - 1, QH * HD - 1].set(edge_value)
    query_vals = query_vals.at[:, STRETCH - 1, QH * HD - 2].set(-edge_value)
    return query_vals.astype(jnp.bfloat16)


def draw_block_rows(key, part):
    keys = jax.random.split(jax.random.fold_in(key, 3), SECTIONS * PANELS)
    orders = jax.vmap(lambda one_key: jax.random.permutation(one_key, NB))(keys)
    return orders[:, :CAP].reshape(SECTIONS, PANELS, CAP).astype(jnp.int32)


def draw_counts(key, part):
    lowest = CAP * 3 // 5
    live_counts = jax.random.randint(jax.random.fold_in(key, 5), (SECTIONS, PANELS), lowest, CAP + 1)
    keys = jax.random.split(jax.random.fold_in(key, 6), SECTIONS)
    orders = jax.vmap(lambda one_key: jax.random.permutation(one_key, PANELS))(keys)
    section_ids = jnp.arange(SECTIONS)
    live_counts = live_counts.at[section_ids, orders[:, 0]].set(CAP)
    live_counts = live_counts.at[section_ids, orders[:, 1]].set(lowest)
    return live_counts.astype(jnp.int32)


def shard_levels(stream_key, extent, cuts, low, high):
    factor_of, own = 1.0, jax.random.fold_in(stream_key, 6)
    for axis_at, blocks in cuts:
        heights = jnp.exp(jax.random.uniform(jax.random.fold_in(own, axis_at), (blocks,), jnp.float32, low / len(cuts), high / len(cuts)))
        factor_of = factor_of * jnp.repeat(heights, extent[axis_at] // blocks).reshape([-1 if axis == axis_at else 1 for axis in range(len(extent))])
    return factor_of


def centred(stream_key, dims, spread, bound, shards=(), kind=jnp.bfloat16):
    values = jax.random.normal(stream_key, dims, jnp.float32) * spread
    if len(shards) > 0:
        values = shard_levels(stream_key, dims, shards, -0.22, 0.18) * values
    return jnp.clip(values, min=-bound, max=bound).astype(kind)


def setup_inputs(seed: int = 0) -> dict:
    key_of = jax.random.split(jax.random.key(seed), 8)
    residual = centred(key_of[0], (SECTIONS, STRETCH, D), 1.0, 6.0, ((0, 16), (1, 32)))
    norm_gain = jnp.clip(1.0 + 0.18 * jax.random.normal(key_of[1], (SECTIONS, D), jnp.float32), 0.099609375, 1.8984375).astype(jnp.bfloat16)
    queries = draw_queries(jax.random.fold_in(key_of[7], 71), 0)
    cached_kv = draw_cached_kv(jax.random.fold_in(key_of[7], 71), 0)
    panel_blocks = centred(key_of[4], (SECTIONS, PANELS * CAP, BLOCK, BLOCK), (D // 2) ** -0.5, 0.125, ((0, 16), (1, 32)))
    block_rows = draw_block_rows(jax.random.fold_in(key_of[7], 71), 0)
    counts = draw_counts(jax.random.fold_in(key_of[7], 71), 0)
    return {"residual": residual, "norm_gain": norm_gain, "queries": queries, "cached_kv": cached_kv, "panel_blocks": panel_blocks, "block_rows": block_rows, "counts": counts}


def rms_rows(stream, gain_row):
    stream_f = stream.astype(jnp.float32)
    scaled = stream_f * lax.rsqrt(lax.optimization_barrier(jnp.mean(stream_f * stream_f, axis=-1, keepdims=True)) + 1e-05)
    return (scaled * gain_row.astype(jnp.float32)).astype(jnp.bfloat16)

def project_section(normed, blocks, row_lists, live_counts):
    stretch_rows = normed.shape[0]
    block_grid = normed.reshape(stretch_rows, D // BLOCK, BLOCK)
    chosen = jnp.take(block_grid, row_lists.reshape(-1).astype(jnp.int32), axis=1)
    slot_out = jnp.einsum('rsk,skn->rsn', chosen.astype(jnp.float32), blocks.astype(jnp.float32))
    live_mask = (jnp.arange(CAP)[None, :] < live_counts[:, None]).astype(jnp.float32).reshape(-1)
    slot_out = slot_out * live_mask[None, :, None]
    summed = slot_out.reshape(stretch_rows, PANELS, CAP, BLOCK).sum(axis=2)
    return summed.reshape(stretch_rows, PANELS * BLOCK).astype(jnp.bfloat16)

def attend_section(query_rows, cache_rows, new_kv):
    every_key = jnp.concatenate([cache_rows, new_kv], axis=0)
    key_pos = jnp.arange(CACHE + STRETCH)
    query_pos = jnp.arange(STRETCH)
    visible = (key_pos[None, :] < CACHE) | (key_pos[None, :] - CACHE <= query_pos[:, None])
    query_grid = query_rows.reshape(STRETCH, KVH, GROUP, HD).astype(jnp.float32)
    score_scale = 1.0 / math.sqrt(HD)
    outputs = []
    for head_idx in range(KVH):
        keys_f = every_key[:, head_idx * HD:(head_idx + 1) * HD].astype(jnp.float32)
        values_f = every_key[:, KVH * HD + head_idx * HD:KVH * HD + (head_idx + 1) * HD].astype(jnp.float32)
        scores = jnp.einsum('rjd,nd->rjn', query_grid[:, head_idx], keys_f) * score_scale
        scores = jnp.where(visible[:, None, :], scores, -jnp.inf)
        row_peak = lax.optimization_barrier(jnp.max(scores, axis=-1, keepdims=True))
        exp_scores = jnp.exp(scores - row_peak)
        denominator = lax.optimization_barrier(jnp.sum(exp_scores, axis=-1, keepdims=True))
        weights_bf = lax.optimization_barrier(exp_scores.astype(jnp.bfloat16)).astype(jnp.float32)
        outputs.append(jnp.einsum('rjn,nd->rjd', weights_bf, values_f) / denominator)
    return jnp.stack(outputs, axis=1).reshape(STRETCH, QH * HD)

def reference(residual, norm_gain, queries, cached_kv, panel_blocks, block_rows, counts):

    def one_section(inputs):
        stream, gain_row, query_rows, cache_rows, blocks, row_lists, live_counts = inputs
        normed = rms_rows(stream, gain_row)
        new_kv = project_section(normed, blocks, row_lists, live_counts)
        attended = attend_section(query_rows, cache_rows, new_kv)
        updated = (stream.astype(jnp.float32) + attended).astype(jnp.bfloat16)
        return (updated, new_kv)
    updated, new_kv = lax.map(one_section, (residual, norm_gain, queries, cached_kv, panel_blocks, block_rows, counts))
    return (jnp.roll(updated, 1, axis=0), new_kv)
```

```python
import math

import jax
import jax.numpy as jnp
from jax import lax
from jax.sharding import PartitionSpec as P

QH = 32
KVH = 4
HD = 128


def passed_along(block, axis, distance):
    devices = range(lax.axis_size(axis))
    route = [((i - distance) % len(devices), i) for i in devices]
    return lax.ppermute(block, axis, route)


def local(residual, norm_gain, queries, cached_kv, panel_blocks, block_rows, counts):
    row_count = residual.shape[1]
    model_width = residual.shape[2]
    zero_index = lax.axis_index("zero")
    stream = residual[0].astype(jnp.float32)
    normed = (
        stream
        * lax.rsqrt(jnp.mean(stream * stream, axis=-1, keepdims=True) + 1e-05)
        * norm_gain[0].astype(jnp.float32)
    ).astype(jnp.bfloat16)
    block_size = panel_blocks.shape[-1]
    panels = block_rows.shape[1]
    slot_depth = block_rows.shape[2]
    row_table = block_rows[0].reshape(-1)
    slot_live = (
        (jnp.arange(slot_depth)[None, :] < counts[0][:, None]).astype(jnp.float32).reshape(-1)
    )
    normed_grid = normed.reshape(row_count, model_width // block_size, block_size)
    kv_heads = KVH
    head_size = HD
    group_size = QH // KVH
    kv_width = kv_heads * head_size
    score_scale = 1.0 / math.sqrt(head_size)
    query_grid = queries[0].reshape(row_count, kv_heads, group_size, head_size)
    first_query = zero_index * row_count
    query_pos = first_query + jnp.arange(row_count)
    initial = (
        jnp.full((kv_heads, row_count, group_size), -1e30, jnp.float32),
        jnp.zeros((kv_heads, row_count, group_size), jnp.float32),
        jnp.zeros((kv_heads, row_count, group_size, head_size), jnp.float32),
    )

    def absorb(running, portion, visible):
        run_max, run_sum, run_acc = running
        key_count = portion.shape[0]
        key_grid = portion[:, :kv_width].reshape(key_count, kv_heads, head_size)
        value_grid = portion[:, kv_width:].reshape(key_count, kv_heads, head_size)
        scores = (
            jnp.einsum("rgjd,ngd->grjn", query_grid, key_grid, preferred_element_type=jnp.float32)
            * score_scale
        )
        visible_mask = visible[None, :, None, :]
        new_max = jnp.maximum(run_max, jnp.max(jnp.where(visible_mask, scores, -1e30), axis=-1))
        shrink = jnp.exp(run_max - new_max)
        weights = jnp.where(visible_mask, jnp.exp(scores - new_max[..., None]), 0.0)
        new_sum = run_sum * shrink + jnp.sum(weights, axis=-1)
        new_acc = run_acc * shrink[..., None] + jnp.einsum(
            "grjn,ngd->grjd",
            weights.astype(jnp.bfloat16),
            value_grid,
            preferred_element_type=jnp.float32,
        )
        return (new_max, new_sum, new_acc)

    zero_size = lax.axis_size("zero")
    local_slots = panel_blocks.shape[1]
    weight_rows = local_slots * block_size
    cache_local = cached_kv[0].reshape(-1, block_size)
    packed = jnp.concatenate([panel_blocks[0].reshape(weight_rows, block_size), cache_local], axis=0)
    gathered = lax.all_gather(packed, "zero", axis=0, tiled=True).reshape(
        zero_size, packed.shape[0], block_size
    )
    all_blocks = gathered[:, :weight_rows].reshape(
        zero_size * local_slots, block_size, block_size
    )
    cache_portion = gathered[:, weight_rows:].reshape(
        zero_size * cached_kv.shape[1], cached_kv.shape[2]
    )
    chosen = jnp.take(normed_grid, row_table, axis=1)
    slot_terms = jnp.einsum(
        "rsk,skn->rsn",
        chosen,
        all_blocks,
        preferred_element_type=jnp.float32,
    )
    slot_terms = slot_terms * slot_live[None, :, None]
    summed = slot_terms.reshape(row_count, panels, slot_depth, block_size).sum(axis=2)
    kv_new = summed.reshape(row_count, panels * block_size).astype(jnp.bfloat16)
    softmax_state = absorb(
        initial, cache_portion, jnp.ones((row_count, cache_portion.shape[0]), bool)
    )
    portion = lax.all_gather(kv_new, "zero", axis=0, tiled=True)
    key_pos = jnp.arange(portion.shape[0])
    visible = key_pos[None, :] <= query_pos[:, None]
    softmax_state = lax.cond(
        jnp.int32(0) <= first_query + row_count - 1,
        lambda state_in: absorb(state_in, portion, visible),
        lambda state_in: state_in,
        softmax_state,
    )
    run_max, denominator, run_acc = softmax_state
    attended = run_acc / denominator[..., None]
    attended = jnp.transpose(attended, (1, 0, 2, 3)).reshape(
        row_count, kv_heads * group_size * head_size
    )
    updated = (stream + attended).astype(jnp.bfloat16)
    passed = passed_along(updated[None], "pipe", 1)
    return (passed, kv_new[None])


def solution(mesh):
    in_specs = (
        P("pipe", "zero", None),
        P("pipe", None),
        P("pipe", "zero", None),
        P("pipe", "zero", None),
        P("pipe", "zero", None, None),
        P("pipe", None, None),
        P("pipe", None),
    )
    out_specs = (P("pipe", "zero", None), P("pipe", "zero", None))
    return jax.shard_map(local, mesh=mesh, in_specs=in_specs, out_specs=out_specs, check_vma=False)
```

```python
import math

import jax
import jax.numpy as jnp
from jax import lax
from jax.sharding import PartitionSpec as P
from jax.experimental import pallas as pl
from jax.experimental.pallas import tpu as pltpu

QH = 32
KVH = 4
HD = 128


def passed_along(block, axis, distance):
    devices = range(lax.axis_size(axis))
    route = [((i - distance) % len(devices), i) for i in devices]
    return lax.ppermute(block, axis, route)


def attend_kernel(first_ref, q_ref, r_ref, ck_ref, cv_ref, nk_ref, nv_ref, o_ref):
    head_size = ck_ref.shape[1]
    rows = q_ref.shape[0]
    new_count = nk_ref.shape[0]
    score_scale = 1.0 / math.sqrt(head_size)
    first = first_ref[0]
    query_pos = first + lax.broadcasted_iota(jnp.int32, (rows, new_count), 0)
    key_pos = lax.broadcasted_iota(jnp.int32, (rows, new_count), 1)
    visible = key_pos <= query_pos
    cache_keys = ck_ref[...]
    new_keys = nk_ref[...]
    cache_values = cv_ref[...]
    new_values = nv_ref[...]
    contract_last = (((1,), (1,)), ((), ()))
    for head in range(q_ref.shape[1] // head_size):
        cols = pl.ds(head * head_size, head_size)
        query = q_ref[:, cols]
        cache_scores = (
            lax.dot_general(query, cache_keys, contract_last, preferred_element_type=jnp.float32)
            * score_scale
        )
        new_scores = (
            lax.dot_general(query, new_keys, contract_last, preferred_element_type=jnp.float32)
            * score_scale
        )
        new_scores = jnp.where(visible, new_scores, -jnp.inf)
        row_max = jnp.maximum(
            jnp.max(cache_scores, axis=-1, keepdims=True),
            jnp.max(new_scores, axis=-1, keepdims=True),
        )
        cache_exp = jnp.exp(cache_scores - row_max)
        new_exp = jnp.exp(new_scores - row_max)
        denominator = jnp.sum(cache_exp, axis=-1, keepdims=True) + jnp.sum(
            new_exp, axis=-1, keepdims=True
        )
        weighted = jnp.dot(
            cache_exp.astype(jnp.bfloat16), cache_values, preferred_element_type=jnp.float32
        ) + jnp.dot(new_exp.astype(jnp.bfloat16), new_values, preferred_element_type=jnp.float32)
        attended = weighted / denominator
        o_ref[:, cols] = (r_ref[:, cols].astype(jnp.float32) + attended).astype(o_ref.dtype)


def attend(first_query, queries, residual, cache_kv, new_kv):
    rows, width = queries.shape
    kv_width = cache_kv.shape[1]
    kv_heads = kv_width // (2 * HD)
    group_width = width // kv_heads
    cache_count = cache_kv.shape[0]
    new_count = new_kv.shape[0]
    keys_total = cache_count + new_count
    grid_spec = pltpu.PrefetchScalarGridSpec(
        num_scalar_prefetch=1,
        grid=(kv_heads,),
        in_specs=[
            pl.BlockSpec((rows, group_width), lambda g, f: (0, g)),
            pl.BlockSpec((rows, group_width), lambda g, f: (0, g)),
            pl.BlockSpec((cache_count, HD), lambda g, f: (0, g)),
            pl.BlockSpec((cache_count, HD), lambda g, f: (0, kv_heads + g)),
            pl.BlockSpec((new_count, HD), lambda g, f: (0, g)),
            pl.BlockSpec((new_count, HD), lambda g, f: (0, kv_heads + g)),
        ],
        out_specs=pl.BlockSpec((rows, group_width), lambda g, f: (0, g)),
    )
    return pl.pallas_call(
        attend_kernel,
        grid_spec=grid_spec,
        out_shape=jax.ShapeDtypeStruct((rows, width), jnp.bfloat16),
        cost_estimate=pl.CostEstimate(
            flops=4 * rows * (width // HD) * keys_total * HD,
            transcendentals=rows * (width // HD) * keys_total,
            bytes_accessed=2 * (3 * rows * width + keys_total * kv_width),
        ),
    )(
        first_query.reshape(1).astype(jnp.int32),
        queries,
        residual,
        cache_kv,
        cache_kv,
        new_kv,
        new_kv,
    )


def local(residual, norm_gain, queries, cached_kv, panel_blocks, block_rows, counts):
    row_count = residual.shape[1]
    model_width = residual.shape[2]
    zero_index = lax.axis_index("zero")
    zero_size = lax.axis_size("zero")
    stream = residual[0].astype(jnp.float32)
    normed = (
        stream
        * lax.rsqrt(jnp.mean(stream * stream, axis=-1, keepdims=True) + 1e-05)
        * norm_gain[0].astype(jnp.float32)
    ).astype(jnp.bfloat16)
    block_size = panel_blocks.shape[-1]
    panels = block_rows.shape[1]
    slot_depth = block_rows.shape[2]
    row_table = block_rows[0].reshape(-1)
    slot_live = (jnp.arange(slot_depth)[None, :] < counts[0][:, None]).reshape(-1)
    normed_grid = normed.reshape(row_count, model_width // block_size, block_size)
    local_slots = panel_blocks.shape[1]
    weight_rows = local_slots * block_size
    cache_local = cached_kv[0].reshape(-1, block_size)
    packed = jnp.concatenate([panel_blocks[0].reshape(weight_rows, block_size), cache_local], axis=0)
    packed_rows = packed.shape[0]
    gathered = lax.all_gather(packed, "zero", axis=0, tiled=True).reshape(
        zero_size, packed_rows, block_size
    )
    cache_portion = gathered[:, weight_rows:].reshape(
        zero_size * cached_kv.shape[1], cached_kv.shape[2]
    )
    chosen = jnp.where(slot_live[None, :, None], jnp.take(normed_grid, row_table, axis=1), 0)
    holders = zero_size // panels
    chosen = chosen.reshape(row_count, panels, holders, weight_rows)
    chosen = jnp.pad(chosen, ((0, 0), (0, 0), (0, 0), (0, packed_rows - weight_rows)))
    kv_new = jnp.einsum(
        "rphk,phkn->rpn",
        chosen,
        gathered.reshape(panels, holders, packed_rows, block_size),
        preferred_element_type=jnp.float32,
    ).reshape(row_count, panels * block_size).astype(jnp.bfloat16)
    portion = lax.all_gather(kv_new, "zero", axis=0, tiled=True)
    updated = attend(zero_index * row_count, queries[0], residual[0], cache_portion, portion)
    passed = passed_along(updated[None], "pipe", 1)
    return (passed, kv_new[None])


def solution(mesh):
    in_specs = (
        P("pipe", "zero", None),
        P("pipe", None),
        P("pipe", "zero", None),
        P("pipe", "zero", None),
        P("pipe", "zero", None, None),
        P("pipe", None, None),
        P("pipe", None),
    )
    out_specs = (P("pipe", "zero", None), P("pipe", "zero", None))
    return jax.shard_map(local, mesh=mesh, in_specs=in_specs, out_specs=out_specs, check_vma=False)
```

```python
import math

import jax
import jax.numpy as jnp
from jax import lax
from jax.sharding import PartitionSpec as P
from jax.experimental import pallas as pl
from jax.experimental.pallas import tpu as pltpu

QH = 32
KVH = 4
HD = 128


def passed_along(block, axis, distance):
    devices = range(lax.axis_size(axis))
    route = [((i - distance) % len(devices), i) for i in devices]
    return lax.ppermute(block, axis, route)


def attend_kernel(first_ref, q_ref, r_ref, ck_ref, cv_ref, nk_ref, nv_ref, o_ref):
    head_size = ck_ref.shape[1]
    rows = q_ref.shape[0]
    new_count = nk_ref.shape[0]
    score_scale = 1.0 / math.sqrt(head_size)
    first = first_ref[0]
    query_pos = first + lax.broadcasted_iota(jnp.int32, (rows, new_count), 0)
    key_pos = lax.broadcasted_iota(jnp.int32, (rows, new_count), 1)
    visible = key_pos <= query_pos
    cache_keys = ck_ref[...]
    new_keys = nk_ref[...]
    cache_values = cv_ref[...]
    new_values = nv_ref[...]
    contract_last = (((1,), (1,)), ((), ()))
    for head in range(q_ref.shape[1] // head_size):
        cols = pl.ds(head * head_size, head_size)
        query = q_ref[:, cols]
        cache_scores = (
            lax.dot_general(query, cache_keys, contract_last, preferred_element_type=jnp.float32)
            * score_scale
        )
        new_scores = (
            lax.dot_general(query, new_keys, contract_last, preferred_element_type=jnp.float32)
            * score_scale
        )
        new_scores = jnp.where(visible, new_scores, -jnp.inf)
        row_max = jnp.maximum(
            jnp.max(cache_scores, axis=-1, keepdims=True),
            jnp.max(new_scores, axis=-1, keepdims=True),
        )
        cache_exp = jnp.exp(cache_scores - row_max)
        new_exp = jnp.exp(new_scores - row_max)
        denominator = jnp.sum(cache_exp, axis=-1, keepdims=True) + jnp.sum(
            new_exp, axis=-1, keepdims=True
        )
        weighted = jnp.dot(
            cache_exp.astype(jnp.bfloat16), cache_values, preferred_element_type=jnp.float32
        ) + jnp.dot(new_exp.astype(jnp.bfloat16), new_values, preferred_element_type=jnp.float32)
        attended = weighted / denominator
        o_ref[:, cols] = (r_ref[:, cols].astype(jnp.float32) + attended).astype(o_ref.dtype)


def attend_group(group, first_query, queries, residual, cache_kv, new_kv):
    rows, width = queries.shape
    kv_width = cache_kv.shape[1]
    kv_heads = kv_width // (2 * HD)
    group_width = width // kv_heads
    cache_count = cache_kv.shape[0]
    new_count = new_kv.shape[0]
    keys_total = cache_count + new_count
    grid_spec = pltpu.PrefetchScalarGridSpec(
        num_scalar_prefetch=1,
        grid=(1,),
        in_specs=[
            pl.BlockSpec((rows, group_width), lambda i, f: (0, group)),
            pl.BlockSpec((rows, group_width), lambda i, f: (0, group)),
            pl.BlockSpec((cache_count, HD), lambda i, f: (0, group)),
            pl.BlockSpec((cache_count, HD), lambda i, f: (0, kv_heads + group)),
            pl.BlockSpec((new_count, HD), lambda i, f: (0, group)),
            pl.BlockSpec((new_count, HD), lambda i, f: (0, kv_heads + group)),
        ],
        out_specs=pl.BlockSpec((rows, group_width), lambda i, f: (0, 0)),
    )
    heads = group_width // HD
    return pl.pallas_call(
        attend_kernel,
        grid_spec=grid_spec,
        out_shape=jax.ShapeDtypeStruct((rows, group_width), jnp.bfloat16),
        cost_estimate=pl.CostEstimate(
            flops=4 * rows * heads * keys_total * HD,
            transcendentals=rows * heads * keys_total,
            bytes_accessed=2 * (3 * rows * group_width + 2 * keys_total * HD),
        ),
    )(
        first_query.reshape(1).astype(jnp.int32),
        queries,
        residual,
        cache_kv,
        cache_kv,
        new_kv,
        new_kv,
    )


def local(residual, norm_gain, queries, cached_kv, panel_blocks, block_rows, counts):
    row_count = residual.shape[1]
    model_width = residual.shape[2]
    zero_index = lax.axis_index("zero")
    zero_size = lax.axis_size("zero")
    stream = residual[0].astype(jnp.float32)
    normed = (
        stream
        * lax.rsqrt(jnp.mean(stream * stream, axis=-1, keepdims=True) + 1e-05)
        * norm_gain[0].astype(jnp.float32)
    ).astype(jnp.bfloat16)
    block_size = panel_blocks.shape[-1]
    panels = block_rows.shape[1]
    slot_depth = block_rows.shape[2]
    row_table = block_rows[0].reshape(-1)
    slot_live = (jnp.arange(slot_depth)[None, :] < counts[0][:, None]).reshape(-1)
    normed_grid = normed.reshape(row_count, model_width // block_size, block_size)
    local_slots = panel_blocks.shape[1]
    weight_rows = local_slots * block_size
    cache_local = cached_kv[0].reshape(-1, block_size)
    packed = jnp.concatenate([panel_blocks[0].reshape(weight_rows, block_size), cache_local], axis=0)
    packed_rows = packed.shape[0]
    gathered = lax.all_gather(packed, "zero", axis=0, tiled=True).reshape(
        zero_size, packed_rows, block_size
    )
    cache_portion = gathered[:, weight_rows:].reshape(
        zero_size * cached_kv.shape[1], cached_kv.shape[2]
    )
    chosen = jnp.where(slot_live[None, :, None], jnp.take(normed_grid, row_table, axis=1), 0)
    holders = zero_size // panels
    chosen = chosen.reshape(row_count, panels, holders, weight_rows)
    chosen = jnp.pad(chosen, ((0, 0), (0, 0), (0, 0), (0, packed_rows - weight_rows)))
    kv_new = jnp.einsum(
        "rphk,phkn->rpn",
        chosen,
        gathered.reshape(panels, holders, packed_rows, block_size),
        preferred_element_type=jnp.float32,
    ).reshape(row_count, panels * block_size).astype(jnp.bfloat16)
    portion = lax.all_gather(kv_new, "zero", axis=0, tiled=True)
    passed = jnp.concatenate(
        [
            passed_along(
                attend_group(
                    group, zero_index * row_count, queries[0], residual[0], cache_portion, portion
                )[None],
                "pipe",
                1,
            )
            for group in range(cached_kv.shape[2] // (2 * HD))
        ],
        axis=-1,
    )
    return (passed, kv_new[None])


def solution(mesh):
    in_specs = (
        P("pipe", "zero", None),
        P("pipe", None),
        P("pipe", "zero", None),
        P("pipe", "zero", None),
        P("pipe", "zero", None, None),
        P("pipe", None, None),
        P("pipe", None),
    )
    out_specs = (P("pipe", "zero", None), P("pipe", "zero", None))
    return jax.shard_map(local, mesh=mesh, in_specs=in_specs, out_specs=out_specs, check_vma=False)
```

```python
import functools
import math

import jax
import jax.numpy as jnp
from jax import lax
from jax.sharding import PartitionSpec as P
from jax.experimental import pallas as pl
from jax.experimental.pallas import tpu as pltpu

QH = 32
KVH = 4
HD = 128


def passed_along(block, axis, distance):
    devices = range(lax.axis_size(axis))
    route = [((i - distance) % len(devices), i) for i in devices]
    return lax.ppermute(block, axis, route)


def attend_kernel(first_ref, pos_ref, q_ref, r_ref, k_ref, v_ref, o_ref, *, stack):
    rows = q_ref.shape[0]
    score_scale = 1.0 / math.sqrt(HD)
    keys = k_ref[...]
    values = v_ref[...]
    key_pos = pos_ref[...]
    stacked = stack * rows
    query_pos = first_ref[0] + jnp.bitwise_and(
        lax.broadcasted_iota(jnp.int32, (stacked, 1), 0), rows - 1
    )
    visible = key_pos <= query_pos
    contract_last = (((1,), (1,)), ((), ()))
    for first_head in range(0, q_ref.shape[1] // HD, stack):
        heads = range(first_head, first_head + stack)
        query = jnp.concatenate([q_ref[:, pl.ds(h * HD, HD)] for h in heads], axis=0)
        scores = (
            lax.dot_general(query, keys, contract_last, preferred_element_type=jnp.float32)
            * score_scale
        )
        scores = jnp.where(visible, scores, -jnp.inf)
        row_max = jnp.max(scores, axis=-1, keepdims=True)
        exp_scores = jnp.exp(scores - row_max)
        denominator = jnp.sum(exp_scores, axis=-1, keepdims=True)
        attended = (
            jnp.dot(exp_scores.astype(jnp.bfloat16), values, preferred_element_type=jnp.float32)
            / denominator
        )
        for i, h in enumerate(heads):
            cols = pl.ds(h * HD, HD)
            o_ref[:, cols] = (
                r_ref[:, cols].astype(jnp.float32) + attended[i * rows : (i + 1) * rows]
            ).astype(o_ref.dtype)


def attend_group(group, first_query, key_pos, queries, residual, every_kv):
    rows, width = queries.shape
    key_count, kv_width = every_kv.shape
    kv_heads = kv_width // (2 * HD)
    group_width = width // kv_heads
    heads = group_width // HD
    grid_spec = pltpu.PrefetchScalarGridSpec(
        num_scalar_prefetch=1,
        grid=(1,),
        in_specs=[
            pl.BlockSpec((1, key_count), lambda i, f: (0, 0)),
            pl.BlockSpec((rows, group_width), lambda i, f: (0, group)),
            pl.BlockSpec((rows, group_width), lambda i, f: (0, group)),
            pl.BlockSpec((key_count, HD), lambda i, f: (0, group)),
            pl.BlockSpec((key_count, HD), lambda i, f: (0, kv_heads + group)),
        ],
        out_specs=pl.BlockSpec((rows, group_width), lambda i, f: (0, 0)),
    )
    return pl.pallas_call(
        functools.partial(attend_kernel, stack=4),
        grid_spec=grid_spec,
        out_shape=jax.ShapeDtypeStruct((rows, group_width), jnp.bfloat16),
        compiler_params=pltpu.CompilerParams(vmem_limit_bytes=48 * 1024 * 1024),
        cost_estimate=pl.CostEstimate(
            flops=4 * rows * heads * key_count * HD,
            transcendentals=rows * heads * key_count,
            bytes_accessed=2 * (3 * rows * group_width + 2 * key_count * HD),
        ),
    )(first_query.reshape(1).astype(jnp.int32), key_pos, queries, residual, every_kv, every_kv)


def local(residual, norm_gain, queries, cached_kv, panel_blocks, block_rows, counts):
    row_count = residual.shape[1]
    model_width = residual.shape[2]
    zero_index = lax.axis_index("zero")
    zero_size = lax.axis_size("zero")
    stream = residual[0].astype(jnp.float32)
    normed = (
        stream
        * lax.rsqrt(jnp.mean(stream * stream, axis=-1, keepdims=True) + 1e-05)
        * norm_gain[0].astype(jnp.float32)
    ).astype(jnp.bfloat16)
    block_size = panel_blocks.shape[-1]
    panels = block_rows.shape[1]
    slot_depth = block_rows.shape[2]
    row_table = block_rows[0].reshape(-1)
    slot_live = (jnp.arange(slot_depth)[None, :] < counts[0][:, None]).reshape(-1)
    normed_grid = normed.reshape(row_count, model_width // block_size, block_size)
    every_block = lax.all_gather(panel_blocks[0], "zero", axis=0, tiled=True)
    chosen = jnp.where(slot_live[None, :, None], jnp.take(normed_grid, row_table, axis=1), 0)
    kv_new = jnp.einsum(
        "rpk,pkn->rpn",
        chosen.reshape(row_count, panels, slot_depth * block_size),
        every_block.reshape(panels, slot_depth * block_size, block_size),
        preferred_element_type=jnp.float32,
    ).reshape(row_count, panels * block_size).astype(jnp.bfloat16)
    cache_rows = cached_kv.shape[1]
    every_kv = lax.all_gather(
        jnp.concatenate([kv_new, cached_kv[0]], axis=0), "zero", axis=0, tiled=True
    )
    piece = jnp.arange(row_count + cache_rows)
    key_pos = jnp.where(
        piece[None, :] < row_count,
        jnp.arange(zero_size)[:, None] * row_count + piece[None, :],
        -1,
    ).reshape(1, -1)
    first_query = zero_index * row_count
    passed = jnp.concatenate(
        [
            passed_along(
                attend_group(group, first_query, key_pos, queries[0], residual[0], every_kv)[None],
                "pipe",
                1,
            )
            for group in range(cached_kv.shape[2] // (2 * HD))
        ],
        axis=-1,
    )
    return (passed, kv_new[None])


def solution(mesh):
    in_specs = (
        P("pipe", "zero", None),
        P("pipe", None),
        P("pipe", "zero", None),
        P("pipe", "zero", None),
        P("pipe", "zero", None, None),
        P("pipe", None, None),
        P("pipe", None),
    )
    out_specs = (P("pipe", "zero", None), P("pipe", "zero", None))
    return jax.shard_map(local, mesh=mesh, in_specs=in_specs, out_specs=out_specs, check_vma=False)
```

```python
import functools
import math

import jax
import jax.numpy as jnp
from jax import lax
from jax.sharding import PartitionSpec as P
from jax.experimental import pallas as pl
from jax.experimental.pallas import tpu as pltpu

QH = 32
KVH = 4
HD = 128


def passed_along(block, axis, distance):
    devices = range(lax.axis_size(axis))
    route = [((i - distance) % len(devices), i) for i in devices]
    return lax.ppermute(block, axis, route)


def attend_kernel(first_ref, pos_ref, q_ref, r_ref, k_ref, v_ref, o_ref, *, stack):
    rows = q_ref.shape[0]
    score_scale = 1.0 / math.sqrt(HD)
    keys = k_ref[...]
    values = v_ref[...]
    key_pos = pos_ref[...]
    stacked = stack * rows
    query_pos = first_ref[0] + jnp.bitwise_and(
        lax.broadcasted_iota(jnp.int32, (stacked, 1), 0), rows - 1
    )
    visible = key_pos <= query_pos
    contract_last = (((1,), (1,)), ((), ()))
    for first_head in range(0, q_ref.shape[1] // HD, stack):
        heads = range(first_head, first_head + stack)
        query = jnp.concatenate([q_ref[:, pl.ds(h * HD, HD)] for h in heads], axis=0)
        scores = (
            lax.dot_general(query, keys, contract_last, preferred_element_type=jnp.float32)
            * score_scale
        )
        scores = jnp.where(visible, scores, -jnp.inf)
        row_max = jnp.max(scores, axis=-1, keepdims=True)
        exp_scores = jnp.exp(scores - row_max)
        denominator = jnp.sum(exp_scores, axis=-1, keepdims=True)
        attended = (
            jnp.dot(exp_scores.astype(jnp.bfloat16), values, preferred_element_type=jnp.float32)
            / denominator
        )
        for i, h in enumerate(heads):
            cols = pl.ds(h * HD, HD)
            o_ref[:, cols] = (
                r_ref[:, cols].astype(jnp.float32) + attended[i * rows : (i + 1) * rows]
            ).astype(o_ref.dtype)


def attend(first_query, key_pos, queries, residual, every_kv):
    rows, width = queries.shape
    key_count, kv_width = every_kv.shape
    kv_heads = kv_width // (2 * HD)
    group_width = width // kv_heads
    grid_spec = pltpu.PrefetchScalarGridSpec(
        num_scalar_prefetch=1,
        grid=(kv_heads,),
        in_specs=[
            pl.BlockSpec((1, key_count), lambda g, f: (0, 0)),
            pl.BlockSpec((rows, group_width), lambda g, f: (0, g)),
            pl.BlockSpec((rows, group_width), lambda g, f: (0, g)),
            pl.BlockSpec((key_count, HD), lambda g, f: (0, g)),
            pl.BlockSpec((key_count, HD), lambda g, f: (0, kv_heads + g)),
        ],
        out_specs=pl.BlockSpec((rows, group_width), lambda g, f: (0, g)),
    )
    return pl.pallas_call(
        functools.partial(attend_kernel, stack=4),
        grid_spec=grid_spec,
        out_shape=jax.ShapeDtypeStruct((rows, width), jnp.bfloat16),
        compiler_params=pltpu.CompilerParams(vmem_limit_bytes=48 * 1024 * 1024),
        cost_estimate=pl.CostEstimate(
            flops=4 * rows * (width // HD) * key_count * HD,
            transcendentals=rows * (width // HD) * key_count,
            bytes_accessed=2 * (3 * rows * width + key_count * kv_width),
        ),
    )(first_query.reshape(1).astype(jnp.int32), key_pos, queries, residual, every_kv, every_kv)


def local(residual, norm_gain, queries, cached_kv, panel_blocks, block_rows, counts):
    row_count = residual.shape[1]
    model_width = residual.shape[2]
    zero_index = lax.axis_index("zero")
    zero_size = lax.axis_size("zero")
    stream = residual[0].astype(jnp.float32)
    normed = (
        stream
        * lax.rsqrt(jnp.mean(stream * stream, axis=-1, keepdims=True) + 1e-05)
        * norm_gain[0].astype(jnp.float32)
    ).astype(jnp.bfloat16)
    block_size = panel_blocks.shape[-1]
    panels = block_rows.shape[1]
    slot_depth = block_rows.shape[2]
    row_table = block_rows[0].reshape(-1)
    slot_live = (jnp.arange(slot_depth)[None, :] < counts[0][:, None]).reshape(-1)
    normed_grid = normed.reshape(row_count, model_width // block_size, block_size)
    every_block = lax.all_gather(panel_blocks[0], "zero", axis=0, tiled=True)
    chosen = jnp.where(slot_live[None, :, None], jnp.take(normed_grid, row_table, axis=1), 0)
    kv_new = jnp.einsum(
        "rpk,pkn->rpn",
        chosen.reshape(row_count, panels, slot_depth * block_size),
        every_block.reshape(panels, slot_depth * block_size, block_size),
        preferred_element_type=jnp.float32,
    ).reshape(row_count, panels * block_size).astype(jnp.bfloat16)
    cache_rows = cached_kv.shape[1]
    every_kv = lax.all_gather(
        jnp.concatenate([kv_new, cached_kv[0]], axis=0), "zero", axis=0, tiled=True
    )
    piece = jnp.arange(row_count + cache_rows)
    key_pos = jnp.where(
        piece[None, :] < row_count,
        jnp.arange(zero_size)[:, None] * row_count + piece[None, :],
        -1,
    ).reshape(1, -1)
    first_query = zero_index * row_count
    updated = attend(first_query, key_pos, queries[0], residual[0], every_kv)
    passed = passed_along(updated[None], "pipe", 1)
    return (passed, kv_new[None])


def solution(mesh):
    in_specs = (
        P("pipe", "zero", None),
        P("pipe", None),
        P("pipe", "zero", None),
        P("pipe", "zero", None),
        P("pipe", "zero", None, None),
        P("pipe", None, None),
        P("pipe", None),
    )
    out_specs = (P("pipe", "zero", None), P("pipe", "zero", None))
    return jax.shard_map(local, mesh=mesh, in_specs=in_specs, out_specs=out_specs, check_vma=False)
```

```python
import functools
import math

import jax
import jax.numpy as jnp
from jax import lax
from jax.sharding import PartitionSpec as P
from jax.experimental import pallas as pl
from jax.experimental.pallas import tpu as pltpu

QH = 32
KVH = 4
HD = 128
PIPE_SPAN = 4


def relay_along(block, axis, span):
    size = lax.axis_size(axis)
    half = block.shape[-1] // 2
    direct_half, relayed_half = block[..., :half], block[..., half:]
    crossing = [p for p in range(size) if p % span == span - 1]
    first = lax.ppermute(direct_half, axis, [(p, (p + 1) % size) for p in range(size)])
    second = lax.ppermute(
        relayed_half, axis, [(p, (p + 1) % size) for p in range(size) if p % span != span - 1]
    )
    leg = lax.ppermute(relayed_half, axis, [(p, p - 1) for p in crossing])
    leg = lax.ppermute(leg, axis, [(p - 1, (p - 1 + span) % size) for p in crossing])
    leg = lax.ppermute(leg, axis, [((p + span) % size - 1, (p + 1) % size) for p in crossing])
    lands = lax.axis_index(axis) % span == 0
    return jnp.concatenate([first, jnp.where(lands, leg, second)], axis=-1)


def passed_along(block, axis, distance):
    devices = range(lax.axis_size(axis))
    route = [((i - distance) % len(devices), i) for i in devices]
    return lax.ppermute(block, axis, route)


def attend_kernel(first_ref, pos_ref, q_ref, r_ref, k_ref, v_ref, o_ref, *, stack):
    rows = q_ref.shape[0]
    score_scale = 1.0 / math.sqrt(HD)
    keys = k_ref[...]
    values = v_ref[...]
    key_pos = pos_ref[...]
    stacked = stack * rows
    query_pos = first_ref[0] + jnp.bitwise_and(
        lax.broadcasted_iota(jnp.int32, (stacked, 1), 0), rows - 1
    )
    visible = key_pos <= query_pos
    contract_last = (((1,), (1,)), ((), ()))
    for first_head in range(0, q_ref.shape[1] // HD, stack):
        heads = range(first_head, first_head + stack)
        query = jnp.concatenate([q_ref[:, pl.ds(h * HD, HD)] for h in heads], axis=0)
        scores = (
            lax.dot_general(query, keys, contract_last, preferred_element_type=jnp.float32)
            * score_scale
        )
        scores = jnp.where(visible, scores, -jnp.inf)
        row_max = jnp.max(scores, axis=-1, keepdims=True)
        exp_scores = jnp.exp(scores - row_max)
        denominator = jnp.sum(exp_scores, axis=-1, keepdims=True)
        attended = (
            jnp.dot(exp_scores.astype(jnp.bfloat16), values, preferred_element_type=jnp.float32)
            / denominator
        )
        for i, h in enumerate(heads):
            cols = pl.ds(h * HD, HD)
            o_ref[:, cols] = (
                r_ref[:, cols].astype(jnp.float32) + attended[i * rows : (i + 1) * rows]
            ).astype(o_ref.dtype)


def attend(first_query, key_pos, queries, residual, every_kv):
    rows, width = queries.shape
    key_count, kv_width = every_kv.shape
    kv_heads = kv_width // (2 * HD)
    group_width = width // kv_heads
    grid_spec = pltpu.PrefetchScalarGridSpec(
        num_scalar_prefetch=1,
        grid=(kv_heads,),
        in_specs=[
            pl.BlockSpec((1, key_count), lambda g, f: (0, 0)),
            pl.BlockSpec((rows, group_width), lambda g, f: (0, g)),
            pl.BlockSpec((rows, group_width), lambda g, f: (0, g)),
            pl.BlockSpec((key_count, HD), lambda g, f: (0, g)),
            pl.BlockSpec((key_count, HD), lambda g, f: (0, kv_heads + g)),
        ],
        out_specs=pl.BlockSpec((rows, group_width), lambda g, f: (0, g)),
    )
    return pl.pallas_call(
        functools.partial(attend_kernel, stack=4),
        grid_spec=grid_spec,
        out_shape=jax.ShapeDtypeStruct((rows, width), jnp.bfloat16),
        compiler_params=pltpu.CompilerParams(vmem_limit_bytes=48 * 1024 * 1024),
        cost_estimate=pl.CostEstimate(
            flops=4 * rows * (width // HD) * key_count * HD,
            transcendentals=rows * (width // HD) * key_count,
            bytes_accessed=2 * (3 * rows * width + key_count * kv_width),
        ),
    )(first_query.reshape(1).astype(jnp.int32), key_pos, queries, residual, every_kv, every_kv)


def local(residual, norm_gain, queries, cached_kv, panel_blocks, block_rows, counts):
    row_count = residual.shape[1]
    model_width = residual.shape[2]
    zero_index = lax.axis_index("zero")
    zero_size = lax.axis_size("zero")
    stream = residual[0].astype(jnp.float32)
    normed = (
        stream
        * lax.rsqrt(jnp.mean(stream * stream, axis=-1, keepdims=True) + 1e-05)
        * norm_gain[0].astype(jnp.float32)
    ).astype(jnp.bfloat16)
    block_size = panel_blocks.shape[-1]
    panels = block_rows.shape[1]
    slot_depth = block_rows.shape[2]
    row_table = block_rows[0].reshape(-1)
    slot_live = (jnp.arange(slot_depth)[None, :] < counts[0][:, None]).reshape(-1)
    normed_grid = normed.reshape(row_count, model_width // block_size, block_size)
    every_block = lax.all_gather(panel_blocks[0], "zero", axis=0, tiled=True)
    chosen = jnp.where(slot_live[None, :, None], jnp.take(normed_grid, row_table, axis=1), 0)
    kv_new = jnp.einsum(
        "rpk,pkn->rpn",
        chosen.reshape(row_count, panels, slot_depth * block_size),
        every_block.reshape(panels, slot_depth * block_size, block_size),
        preferred_element_type=jnp.float32,
    ).reshape(row_count, panels * block_size).astype(jnp.bfloat16)
    cache_rows = cached_kv.shape[1]
    every_kv = lax.all_gather(
        jnp.concatenate([kv_new, cached_kv[0]], axis=0), "zero", axis=0, tiled=True
    )
    piece = jnp.arange(row_count + cache_rows)
    key_pos = jnp.where(
        piece[None, :] < row_count,
        jnp.arange(zero_size)[:, None] * row_count + piece[None, :],
        -1,
    ).reshape(1, -1)
    first_query = zero_index * row_count
    updated = attend(first_query, key_pos, queries[0], residual[0], every_kv)
    passed = relay_along(updated[None], "pipe", PIPE_SPAN)
    return (passed, kv_new[None])


def solution(mesh):
    in_specs = (
        P("pipe", "zero", None),
        P("pipe", None),
        P("pipe", "zero", None),
        P("pipe", "zero", None),
        P("pipe", "zero", None, None),
        P("pipe", None, None),
        P("pipe", None),
    )
    out_specs = (P("pipe", "zero", None), P("pipe", "zero", None))
    return jax.shard_map(local, mesh=mesh, in_specs=in_specs, out_specs=out_specs, check_vma=False)
```

```python
import functools
import math

import jax
import jax.numpy as jnp
from jax import lax
from jax.sharding import PartitionSpec as P
from jax.experimental import pallas as pl
from jax.experimental.pallas import tpu as pltpu

QH = 32
KVH = 4
HD = 128
PIPE_SPAN = 4


def relay_along(block, axis, span):
    size = lax.axis_size(axis)
    half = block.shape[-1] // 2
    direct_half, relayed_half = block[..., :half], block[..., half:]
    crossing = [p for p in range(size) if p % span == span - 1]
    first = lax.ppermute(direct_half, axis, [(p, (p + 1) % size) for p in range(size)])
    second = lax.ppermute(
        relayed_half,
        axis,
        [(p, (p + 1) % size) for p in range(size) if p % span != span - 1]
        + [(p, p + 1 - span) for p in crossing],
    )
    leg = lax.ppermute(second, axis, [(p + 1 - span, (p + 1) % size) for p in crossing])
    lands = lax.axis_index(axis) % span == 0
    return jnp.concatenate([first, jnp.where(lands, leg, second)], axis=-1)


def passed_along(block, axis, distance):
    devices = range(lax.axis_size(axis))
    route = [((i - distance) % len(devices), i) for i in devices]
    return lax.ppermute(block, axis, route)


def attend_kernel(first_ref, pos_ref, q_ref, r_ref, k_ref, v_ref, o_ref, *, stack):
    rows = q_ref.shape[0]
    score_scale = 1.0 / math.sqrt(HD)
    keys = k_ref[...]
    values = v_ref[...]
    key_pos = pos_ref[...]
    stacked = stack * rows
    query_pos = first_ref[0] + jnp.bitwise_and(
        lax.broadcasted_iota(jnp.int32, (stacked, 1), 0), rows - 1
    )
    visible = key_pos <= query_pos
    contract_last = (((1,), (1,)), ((), ()))
    for first_head in range(0, q_ref.shape[1] // HD, stack):
        heads = range(first_head, first_head + stack)
        query = jnp.concatenate([q_ref[:, pl.ds(h * HD, HD)] for h in heads], axis=0)
        scores = (
            lax.dot_general(query, keys, contract_last, preferred_element_type=jnp.float32)
            * score_scale
        )
        scores = jnp.where(visible, scores, -jnp.inf)
        row_max = jnp.max(scores, axis=-1, keepdims=True)
        exp_scores = jnp.exp(scores - row_max)
        denominator = jnp.sum(exp_scores, axis=-1, keepdims=True)
        attended = (
            jnp.dot(exp_scores.astype(jnp.bfloat16), values, preferred_element_type=jnp.float32)
            / denominator
        )
        for i, h in enumerate(heads):
            cols = pl.ds(h * HD, HD)
            o_ref[:, cols] = (
                r_ref[:, cols].astype(jnp.float32) + attended[i * rows : (i + 1) * rows]
            ).astype(o_ref.dtype)


def attend(first_query, key_pos, queries, residual, every_kv):
    rows, width = queries.shape
    key_count, kv_width = every_kv.shape
    kv_heads = kv_width // (2 * HD)
    group_width = width // kv_heads
    grid_spec = pltpu.PrefetchScalarGridSpec(
        num_scalar_prefetch=1,
        grid=(kv_heads,),
        in_specs=[
            pl.BlockSpec((1, key_count), lambda g, f: (0, 0)),
            pl.BlockSpec((rows, group_width), lambda g, f: (0, g)),
            pl.BlockSpec((rows, group_width), lambda g, f: (0, g)),
            pl.BlockSpec((key_count, HD), lambda g, f: (0, g)),
            pl.BlockSpec((key_count, HD), lambda g, f: (0, kv_heads + g)),
        ],
        out_specs=pl.BlockSpec((rows, group_width), lambda g, f: (0, g)),
    )
    return pl.pallas_call(
        functools.partial(attend_kernel, stack=4),
        grid_spec=grid_spec,
        out_shape=jax.ShapeDtypeStruct((rows, width), jnp.bfloat16),
        compiler_params=pltpu.CompilerParams(vmem_limit_bytes=48 * 1024 * 1024),
        cost_estimate=pl.CostEstimate(
            flops=4 * rows * (width // HD) * key_count * HD,
            transcendentals=rows * (width // HD) * key_count,
            bytes_accessed=2 * (3 * rows * width + key_count * kv_width),
        ),
    )(first_query.reshape(1).astype(jnp.int32), key_pos, queries, residual, every_kv, every_kv)


def local(residual, norm_gain, queries, cached_kv, panel_blocks, block_rows, counts):
    row_count = residual.shape[1]
    model_width = residual.shape[2]
    zero_index = lax.axis_index("zero")
    zero_size = lax.axis_size("zero")
    stream = residual[0].astype(jnp.float32)
    normed = (
        stream
        * lax.rsqrt(jnp.mean(stream * stream, axis=-1, keepdims=True) + 1e-05)
        * norm_gain[0].astype(jnp.float32)
    ).astype(jnp.bfloat16)
    block_size = panel_blocks.shape[-1]
    panels = block_rows.shape[1]
    slot_depth = block_rows.shape[2]
    row_table = block_rows[0].reshape(-1)
    slot_live = (jnp.arange(slot_depth)[None, :] < counts[0][:, None]).reshape(-1)
    normed_grid = normed.reshape(row_count, model_width // block_size, block_size)
    every_block = lax.all_gather(panel_blocks[0], "zero", axis=0, tiled=True)
    chosen = jnp.where(slot_live[None, :, None], jnp.take(normed_grid, row_table, axis=1), 0)
    kv_new = jnp.einsum(
        "rpk,pkn->rpn",
        chosen.reshape(row_count, panels, slot_depth * block_size),
        every_block.reshape(panels, slot_depth * block_size, block_size),
        preferred_element_type=jnp.float32,
    ).reshape(row_count, panels * block_size).astype(jnp.bfloat16)
    cache_rows = cached_kv.shape[1]
    every_kv = lax.all_gather(
        jnp.concatenate([kv_new, cached_kv[0]], axis=0), "zero", axis=0, tiled=True
    )
    piece = jnp.arange(row_count + cache_rows)
    key_pos = jnp.where(
        piece[None, :] < row_count,
        jnp.arange(zero_size)[:, None] * row_count + piece[None, :],
        -1,
    ).reshape(1, -1)
    first_query = zero_index * row_count
    updated = attend(first_query, key_pos, queries[0], residual[0], every_kv)
    passed = relay_along(updated[None], "pipe", PIPE_SPAN)
    return (passed, kv_new[None])


def solution(mesh):
    in_specs = (
        P("pipe", "zero", None),
        P("pipe", None),
        P("pipe", "zero", None),
        P("pipe", "zero", None),
        P("pipe", "zero", None, None),
        P("pipe", None, None),
        P("pipe", None),
    )
    out_specs = (P("pipe", "zero", None), P("pipe", "zero", None))
    return jax.shard_map(local, mesh=mesh, in_specs=in_specs, out_specs=out_specs, check_vma=False)
```

```python
import functools
import math

import jax
import jax.numpy as jnp
from jax import lax
from jax.sharding import PartitionSpec as P
from jax.experimental import pallas as pl
from jax.experimental.pallas import tpu as pltpu

QH = 32
KVH = 4
HD = 128
PIPE_SPAN = 4


def relay_along(block, axis, span):
    size = lax.axis_size(axis)
    half = block.shape[-1] // 2
    direct_half, relayed_half = block[..., :half], block[..., half:]
    crossing = [p for p in range(size) if p % span == span - 1]
    first = lax.ppermute(direct_half, axis, [(p, (p + 1) % size) for p in range(size)])
    second = lax.ppermute(
        relayed_half,
        axis,
        [(p, (p + 1) % size) for p in range(size) if p % span != span - 1]
        + [(p, p + 1 - span) for p in crossing],
    )
    leg = lax.ppermute(second, axis, [(p + 1 - span, (p + 1) % size) for p in crossing])
    lands = lax.axis_index(axis) % span == 0
    return jnp.concatenate([first, jnp.where(lands, leg, second)], axis=-1)


def passed_along(block, axis, distance):
    devices = range(lax.axis_size(axis))
    route = [((i - distance) % len(devices), i) for i in devices]
    return lax.ppermute(block, axis, route)


def attend_kernel(first_ref, pos_ref, q_ref, r_ref, k_ref, v_ref, o_ref, *, stack):
    rows = q_ref.shape[0]
    score_scale = 1.0 / math.sqrt(HD)
    keys = k_ref[...]
    values = v_ref[...]
    key_pos = pos_ref[...]
    stacked = stack * rows
    query_pos = first_ref[0] + jnp.bitwise_and(
        lax.broadcasted_iota(jnp.int32, (stacked, 1), 0), rows - 1
    )
    visible = key_pos <= query_pos
    contract_last = (((1,), (1,)), ((), ()))
    for first_head in range(0, q_ref.shape[1] // HD, stack):
        heads = range(first_head, first_head + stack)
        query = jnp.concatenate([q_ref[:, pl.ds(h * HD, HD)] for h in heads], axis=0)
        scores = (
            lax.dot_general(query, keys, contract_last, preferred_element_type=jnp.float32)
            * score_scale
        )
        scores = jnp.where(visible, scores, -jnp.inf)
        row_max = jnp.max(scores, axis=-1, keepdims=True)
        exp_scores = jnp.exp(scores - row_max)
        denominator = jnp.sum(exp_scores, axis=-1, keepdims=True)
        attended = (
            jnp.dot(exp_scores.astype(jnp.bfloat16), values, preferred_element_type=jnp.float32)
            / denominator
        )
        for i, h in enumerate(heads):
            cols = pl.ds(h * HD, HD)
            o_ref[:, cols] = (
                r_ref[:, cols].astype(jnp.float32) + attended[i * rows : (i + 1) * rows]
            ).astype(o_ref.dtype)


def attend(first_query, key_pos, queries, residual, every_kv):
    rows, width = queries.shape
    key_count, kv_width = every_kv.shape
    kv_heads = kv_width // (2 * HD)
    group_width = width // kv_heads
    grid_spec = pltpu.PrefetchScalarGridSpec(
        num_scalar_prefetch=1,
        grid=(kv_heads,),
        in_specs=[
            pl.BlockSpec((1, key_count), lambda g, f: (0, 0)),
            pl.BlockSpec((rows, group_width), lambda g, f: (0, g)),
            pl.BlockSpec((rows, group_width), lambda g, f: (0, g)),
            pl.BlockSpec((key_count, HD), lambda g, f: (0, g)),
            pl.BlockSpec((key_count, HD), lambda g, f: (0, kv_heads + g)),
        ],
        out_specs=pl.BlockSpec((rows, group_width), lambda g, f: (0, g)),
    )
    return pl.pallas_call(
        functools.partial(attend_kernel, stack=8),
        grid_spec=grid_spec,
        out_shape=jax.ShapeDtypeStruct((rows, width), jnp.bfloat16),
        compiler_params=pltpu.CompilerParams(vmem_limit_bytes=48 * 1024 * 1024),
        cost_estimate=pl.CostEstimate(
            flops=4 * rows * (width // HD) * key_count * HD,
            transcendentals=rows * (width // HD) * key_count,
            bytes_accessed=2 * (3 * rows * width + key_count * kv_width),
        ),
    )(first_query.reshape(1).astype(jnp.int32), key_pos, queries, residual, every_kv, every_kv)


def local(residual, norm_gain, queries, cached_kv, panel_blocks, block_rows, counts):
    row_count = residual.shape[1]
    model_width = residual.shape[2]
    zero_index = lax.axis_index("zero")
    zero_size = lax.axis_size("zero")
    stream = residual[0].astype(jnp.float32)
    normed = (
        stream
        * lax.rsqrt(jnp.mean(stream * stream, axis=-1, keepdims=True) + 1e-05)
        * norm_gain[0].astype(jnp.float32)
    ).astype(jnp.bfloat16)
    block_size = panel_blocks.shape[-1]
    panels = block_rows.shape[1]
    slot_depth = block_rows.shape[2]
    row_table = block_rows[0].reshape(-1)
    slot_live = (jnp.arange(slot_depth)[None, :] < counts[0][:, None]).reshape(-1)
    normed_grid = normed.reshape(row_count, model_width // block_size, block_size)
    every_block = lax.all_gather(panel_blocks[0], "zero", axis=0, tiled=True)
    chosen = jnp.where(slot_live[None, :, None], jnp.take(normed_grid, row_table, axis=1), 0)
    kv_new = jnp.einsum(
        "rpk,pkn->rpn",
        chosen.reshape(row_count, panels, slot_depth * block_size),
        every_block.reshape(panels, slot_depth * block_size, block_size),
        preferred_element_type=jnp.float32,
    ).reshape(row_count, panels * block_size).astype(jnp.bfloat16)
    cache_rows = cached_kv.shape[1]
    every_kv = lax.all_gather(
        jnp.concatenate([kv_new, cached_kv[0]], axis=0), "zero", axis=0, tiled=True
    )
    piece = jnp.arange(row_count + cache_rows)
    key_pos = jnp.where(
        piece[None, :] < row_count,
        jnp.arange(zero_size)[:, None] * row_count + piece[None, :],
        -1,
    ).reshape(1, -1)
    first_query = zero_index * row_count
    updated = attend(first_query, key_pos, queries[0], residual[0], every_kv)
    passed = relay_along(updated[None], "pipe", PIPE_SPAN)
    return (passed, kv_new[None])


def solution(mesh):
    in_specs = (
        P("pipe", "zero", None),
        P("pipe", None),
        P("pipe", "zero", None),
        P("pipe", "zero", None),
        P("pipe", "zero", None, None),
        P("pipe", None, None),
        P("pipe", None),
    )
    out_specs = (P("pipe", "zero", None), P("pipe", "zero", None))
    return jax.shard_map(local, mesh=mesh, in_specs=in_specs, out_specs=out_specs, check_vma=False)
```
